512 devices in a mesh: seq: 32 (over z_lo, y), tensor: 8 (over z_hi, x), enc: 2 (over core).
Axes of the slice: x: 4, y: 4, z: 16 (z_hi: 2, z_lo: 8; z = z_hi * 8 + z_lo), core: 2. Of those that a mesh axis runs over, the one named last changes fastest.
Arguments:
- neighbour_rows: bfloat16 [32768, 1024], P('seq'), may hold values from -17 to 17
- norm_gain: float32 [1024], replicated, may hold values from 0.1 to 1.9
- up_weight: bfloat16 [1024, 4096], P(None, ('tensor', 'enc')), may hold values from -0.1875 to 0.1875
- down_weight: bfloat16 [4096, 1024], P(('tensor', 'enc')), may hold values from -0.09375 to 0.09375
- final_gain: float32 [1024], replicated, may hold values from 0.1 to 1.9
- key_weight: bfloat16 [1024, 4096], P(None, ('tensor', 'enc')), may hold values from -0.1875 to 0.1875
- value_weight: bfloat16 [1024, 4096], P(None, ('tensor', 'enc')), may hold values from -0.1875 to 0.1875
- queries: bfloat16 [32768, 4096], P('seq', ('tensor', 'enc')), may hold values from -170 to 170
- block_lists: int32 [512, 2], P('seq'), may hold values from 0 to 255, as said below
- live_counts: int32 [512], P('seq'), may hold values from 1 to 2
Outputs:
- attended: bfloat16 [32768, 4096], P('seq', ('tensor', 'enc'))
The draws below stay inside these ranges and needn't reach their ends.
Inputs may be any that keep to these rules, and one draw needn't show every extreme that they name: `block_lists`: block b of the pool lies on the device of index b // 8 along seq. The two entries of a span name blocks of two different devices. Among all list entries of one device's spans (those beyond a span's count included) at most 1 name blocks of any one device, and in every draw some device's entries reach 1 for some device.
All inputs are finite; a program needn't handle non-finite values.
Results may differ from the reference program's by a relative error of at most 0.019.
The reference program's roundings to bfloat16 on the way (of `normed`, `hidden`, `final_rows`, `key_rows`, `value_rows` and `rounded`) count: a program that leaves them out, or rounds other values in their place, can miss the bound.
Values may be sent and summed in bfloat16 or wider, within the bound.
No kernel may reach another device: no remote copies, remote signals or barrier semaphores. Data moves between devices by JAX's collectives and lax.ppermute only.
A program may use at most 64 MiB of HBM per device.

```python
import math
import jax
import jax.numpy as jnp
from jax import lax

DE = 1024
FFE = 4096
H = 32
DH = 128
NB = 128
CL = 64
KMAX = 2
C_DEV = 16
B_DEV = 8
SPANS = 512
POOL = 256
TOKENS = 32768
POOL_ROWS = 32768
N_SEQ = 32


def draw_neighbour_rows(key, part):
    first = jax.random.fold_in(key, 0)
    array_shape = (POOL_ROWS, DE)
    return jnp.clip(jax.random.normal(first, array_shape, jnp.float32), -6.0, 6.0).astype(jnp.bfloat16)


def draw_queries(key, part):
    first = jax.random.fold_in(key, 0)
    array_shape = (TOKENS, H * DH)
    return jnp.clip(jax.random.normal(first, array_shape, jnp.float32), -6.0, 6.0).astype(jnp.bfloat16)


def draw_block_lists(key, part):
    devices = SPANS // C_DEV
    need_count = C_DEV * KMAX
    key_list = jax.random.split(jax.random.fold_in(key, 7), devices)
    orders = jax.vmap(lambda single: jax.random.permutation(single, devices))(key_list)
    position = jnp.arange(need_count) % devices
    owners = orders[:, position]
    first_pick = jax.random.randint(jax.random.fold_in(key, 11), (devices, need_count), 0, B_DEV)
    second_pick = jax.random.randint(jax.random.fold_in(key, 13), (devices, need_count), 0, B_DEV)
    local_index = jnp.minimum(first_pick, second_pick)
    return (owners * B_DEV + local_index).reshape(SPANS, KMAX).astype(jnp.int32)


def set_ends(entries, key, smallest, top_value):
    longest = entries.shape.index(max(entries.shape))
    spots = []
    for shift in (0, 1):
        where = [jax.random.randint(jax.random.fold_in(key, axis), (), 0, length) for axis, length in enumerate(entries.shape)]
        where[longest] = (where[longest] + shift) % entries.shape[longest]
        spots.append(tuple(where))
    return entries.at[spots[0]].set(smallest).at[spots[1]].set(top_value)


def block_levels(own_key, extent, shards, least, largest):
    level = 1.0
    for axis_at, parts in shards:
        heights = jax.random.uniform(jax.random.fold_in(jax.random.fold_in(own_key, 6), axis_at), (parts,), jnp.float32, least / len(shards), largest / len(shards))
        level = level * jnp.repeat(jnp.exp(heights), extent[axis_at] // parts).reshape((-1,) + (1,) * (len(extent) - 1 - axis_at))
    return level


def centred(rng, shape, width, reach, pieces=(), dtype=jnp.bfloat16):
    loudness = block_levels(rng, shape, pieces, -0.22, 0.18) if pieces else 1.0
    values = jax.random.normal(rng, shape, jnp.float32) * width * loudness
    return jnp.minimum(jnp.maximum(values, -reach), reach).astype(dtype)


def setup_inputs(seed: int = 0) -> dict:
    key_of = jax.random.split(jax.random.key(seed), 11)
    return {
        "neighbour_rows": draw_neighbour_rows(jax.random.fold_in(key_of[10], 71), 0),
        "norm_gain": jnp.clip(1.0 + 0.18 * jax.random.normal(key_of[1], (DE,), jnp.float32), 0.1, 1.9),
        "up_weight": centred(key_of[2], (DE, FFE), DE ** -0.5, 0.1875, ((1, 16),)),
        "down_weight": centred(key_of[3], (FFE, DE), FFE ** -0.5, 0.09375, ((0, 16),)),
        "final_gain": jnp.clip(1.0 + 0.18 * jax.random.normal(key_of[4], (DE,), jnp.float32), 0.1, 1.9),
        "key_weight": centred(key_of[5], (DE, H * DH), DE ** -0.5, 0.1875, ((1, 16),)),
        "value_weight": centred(key_of[6], (DE, H * DH), DE ** -0.5, 0.1875, ((1, 16),)),
        "queries": draw_queries(jax.random.fold_in(key_of[10], 71), 0),
        "block_lists": draw_block_lists(jax.random.fold_in(key_of[10], 71), 0),
        "live_counts": set_ends(jax.random.randint(key_of[9], (SPANS,), 1, KMAX + 1), jax.random.fold_in(key_of[9], 1), 1, KMAX).astype(jnp.int32),
    }


def rms_scale(rows, gain):
    mean_square = lax.optimization_barrier(jnp.mean(rows * rows, axis=-1, keepdims=True))
    return rows * lax.rsqrt(mean_square + 1e-06) * gain

def reference(neighbour_rows, norm_gain, up_weight, down_weight, final_gain, key_weight, value_weight, queries, block_lists, live_counts):

    def encode(rows):
        widened = rows.astype(jnp.float32)
        normed = rms_scale(widened, norm_gain).astype(jnp.bfloat16)
        hidden = jax.nn.gelu(jnp.dot(normed, up_weight, preferred_element_type=jnp.float32)).astype(jnp.bfloat16)
        encoded = widened + jnp.dot(hidden, down_weight, preferred_element_type=jnp.float32)
        final_rows = rms_scale(encoded, final_gain).astype(jnp.bfloat16)
        key_part = jnp.dot(final_rows, key_weight, preferred_element_type=jnp.float32).astype(jnp.bfloat16)
        value_part = jnp.dot(final_rows, value_weight, preferred_element_type=jnp.float32).astype(jnp.bfloat16)
        return (key_part, value_part)
    grouped = neighbour_rows.reshape(N_SEQ, B_DEV * NB, DE)
    key_rows, value_rows = lax.map(encode, grouped)
    key_blocks = key_rows.reshape(POOL, NB, H * DH)
    value_blocks = value_rows.reshape(POOL, NB, H * DH)

    def attend(operands):
        query_rows, lists, counts = operands
        query_tiles = query_rows.astype(jnp.float32).reshape(C_DEV, CL, H, DH)
        flat_lists = lists.reshape(C_DEV * KMAX).astype(jnp.int32)
        key_tiles = jnp.take(key_blocks, flat_lists, axis=0).astype(jnp.float32).reshape(C_DEV, KMAX * NB, H, DH)
        value_tiles = jnp.take(value_blocks, flat_lists, axis=0).astype(jnp.float32).reshape(C_DEV, KMAX * NB, H, DH)
        scores = jnp.einsum('cqhd,ckhd->chqk', query_tiles, key_tiles) / math.sqrt(DH)
        live_mask = jnp.arange(KMAX)[None, :] < counts[:, None]
        key_mask = jnp.repeat(live_mask, NB, axis=1)
        scores = jnp.where(key_mask[:, None, None, :], scores, -1e+30)
        highest = lax.optimization_barrier(jnp.max(scores, axis=-1, keepdims=True))
        weights = jnp.exp(scores - highest)
        row_total = lax.optimization_barrier(jnp.sum(weights, axis=-1))
        rounded = lax.optimization_barrier(weights.astype(jnp.bfloat16)).astype(jnp.float32)
        summed = jnp.einsum('chqk,ckhd->cqhd', rounded, value_tiles)
        result = summed / jnp.transpose(row_total, (0, 2, 1))[..., None]
        return result.reshape(C_DEV * CL, H * DH).astype(jnp.bfloat16)
    attended = lax.map(attend, (queries.reshape(N_SEQ, C_DEV * CL, H * DH), block_lists.reshape(N_SEQ, C_DEV, KMAX), live_counts.reshape(N_SEQ, C_DEV)))
    return attended.reshape(TOKENS, H * DH)
```

```python
import math

import jax
import jax.numpy as jnp
from jax import lax
from jax.sharding import PartitionSpec as P

DH = 128
NB = 128
CL = 64
KMAX = 2
TAG = 128


def rms_scale(rows, gain):
    mean_square = jnp.mean(rows * rows, axis=-1, keepdims=True)
    return rows * lax.rsqrt(mean_square + 1e-06) * gain


def need_ranks(owners):
    need_count = owners.shape[-1]
    order_index = jnp.arange(need_count)
    same_owner = owners[..., :, None] == owners[..., None, :]
    earlier = order_index[None, :] < order_index[:, None]
    return jnp.sum(jnp.logical_and(same_owner, earlier), axis=-1)


def shards(
    neighbour_rows,
    norm_gain,
    up_weight,
    down_weight,
    final_gain,
    key_weight,
    value_weight,
    queries,
    block_lists,
    live_counts,
):
    block_rows = neighbour_rows.shape[0]
    blocks = block_rows // NB
    head_width = key_weight.shape[1]
    heads_local = head_width // DH
    seq_count = lax.axis_size("seq")
    span_count = live_counts.shape[0]
    need_count = span_count * KMAX
    capacity = (need_count + seq_count - 1) // seq_count
    slots = seq_count * capacity
    q_width = CL * head_width

    flat_lists = block_lists.reshape(need_count)
    owners = flat_lists // blocks
    rank_order = need_ranks(owners)
    slot_index = owners * capacity + rank_order
    slot_range = jnp.arange(slots)
    slot_match = slot_index[None, :] == slot_range[:, None]
    entry_of_slot = jnp.sum(jnp.where(slot_match, jnp.arange(need_count)[None, :], 0), axis=1)
    filled = jnp.any(slot_match, axis=1)
    span_of_slot = entry_of_slot // KMAX
    block_of_slot = jnp.where(filled, flat_lists[entry_of_slot] % blocks, 0)
    span_queries = queries.reshape(span_count, q_width)
    sent_queries = jnp.take(span_queries, span_of_slot, axis=0)
    sent_queries = jnp.where(filled[:, None], sent_queries, jnp.zeros((), jnp.bfloat16))
    tag = jnp.broadcast_to(block_of_slot.astype(jnp.bfloat16)[:, None], (slots, TAG))
    outgoing = jnp.concatenate([sent_queries, tag], axis=1)
    incoming = lax.all_to_all(outgoing, "seq", split_axis=0, concat_axis=0, tiled=True)

    widened = neighbour_rows.astype(jnp.float32)
    normed = rms_scale(widened, norm_gain).astype(jnp.bfloat16)
    hidden = jax.nn.gelu(jnp.dot(normed, up_weight, preferred_element_type=jnp.float32)).astype(
        jnp.bfloat16
    )
    partial_sum = jnp.dot(hidden, down_weight, preferred_element_type=jnp.float32)
    reduced = lax.psum_scatter(partial_sum, ("tensor", "enc"), scatter_dimension=0, tiled=True)
    piece_rows = reduced.shape[0]
    piece = lax.axis_index("tensor") * lax.axis_size("enc") + lax.axis_index("enc")
    own_rows = lax.dynamic_slice_in_dim(neighbour_rows, piece * piece_rows, piece_rows, axis=0)
    encoded = own_rows.astype(jnp.float32) + reduced
    final_piece = rms_scale(encoded, final_gain).astype(jnp.bfloat16)
    final_rows = lax.all_gather(final_piece, ("tensor", "enc"), axis=0, tiled=True)
    key_part = jnp.dot(final_rows, key_weight, preferred_element_type=jnp.float32).astype(
        jnp.bfloat16
    )
    value_part = jnp.dot(final_rows, value_weight, preferred_element_type=jnp.float32).astype(
        jnp.bfloat16
    )
    key_blocks = key_part.reshape(blocks, NB, heads_local, DH)
    value_blocks = value_part.reshape(blocks, NB, heads_local, DH)

    in_queries = incoming[:, :q_width].reshape(slots, CL, heads_local, DH)
    in_block = incoming[:, q_width].astype(jnp.int32)
    in_block = jnp.clip(in_block, 0, blocks - 1)
    key_tiles = jnp.take(key_blocks, in_block, axis=0)
    value_tiles = jnp.take(value_blocks, in_block, axis=0)
    scores = jnp.einsum(
        "sqhd,skhd->shqk", in_queries, key_tiles, preferred_element_type=jnp.float32
    ) / math.sqrt(DH)
    local_max = jnp.max(scores, axis=-1, keepdims=True)
    weights = jnp.exp(scores - local_max)
    local_total = jnp.sum(weights, axis=-1)
    summed = jnp.einsum(
        "shqk,skhd->sqhd",
        weights.astype(jnp.bfloat16),
        value_tiles,
        preferred_element_type=jnp.float32,
    )
    stats = jnp.concatenate(
        [local_max[..., 0].reshape(slots, -1), local_total.reshape(slots, -1)], axis=1
    )
    reply = jnp.concatenate([summed.reshape(slots, q_width), stats], axis=1)
    returned = lax.all_to_all(reply, "seq", split_axis=0, concat_axis=0, tiled=True)

    stat_width = heads_local * CL
    picked = jnp.take(returned, slot_index, axis=0).reshape(span_count, KMAX, -1)
    part_sum = picked[..., :q_width].reshape(span_count, KMAX, CL, heads_local, DH)
    part_max = picked[..., q_width : q_width + stat_width].reshape(
        span_count, KMAX, heads_local, CL
    )
    part_total = picked[..., q_width + stat_width :].reshape(span_count, KMAX, heads_local, CL)
    live_mask = (jnp.arange(KMAX)[None, :] < live_counts[:, None])[:, :, None, None]
    part_max = jnp.where(live_mask, part_max, -jnp.inf)
    highest = jnp.max(part_max, axis=1, keepdims=True)
    scale = jnp.where(live_mask, jnp.exp(part_max - highest), 0.0)
    row_total = jnp.sum(scale * part_total, axis=1)
    scale_rows = jnp.transpose(scale, (0, 1, 3, 2))[..., None]
    combined = jnp.sum(jnp.where(scale_rows > 0, scale_rows * part_sum, 0.0), axis=1)
    result = combined / jnp.transpose(row_total, (0, 2, 1))[..., None]
    return result.reshape(span_count * CL, head_width).astype(jnp.bfloat16)


def solution(mesh):
    placed = (
        P("seq", None),
        P(),
        P(None, ("tensor", "enc")),
        P(("tensor", "enc"), None),
        P(),
        P(None, ("tensor", "enc")),
        P(None, ("tensor", "enc")),
        P("seq", ("tensor", "enc")),
        P("seq", None),
        P("seq"),
    )
    return jax.shard_map(
        shards, mesh=mesh, in_specs=placed, out_specs=P("seq", ("tensor", "enc")), check_vma=False
    )
```
